128 devices in a mesh: row: 8 (over x_hi, z), col: 16 (over y, x_lo, core).
Axes of the slice: x: 4 (x_hi: 2, x_lo: 2; x = x_hi * 2 + x_lo), y: 4, z: 4, core: 2. Of those that a mesh axis runs over, the one named last changes fastest.
Arguments:
- residual: bfloat16 [1024, 16384], P('col', 'row'), may hold values from -16 to 16
- norm_gain: float32 [16384], P('row'), may hold values from 0.5 to 1.5
- query_weight: bfloat16 [16384, 16384], P('row', 'col'), may hold values from -0.046875 to 0.046875
- key_weight: bfloat16 [16384, 1024], P('row', 'col'), may hold values from -0.09375 to 0.09375
- value_weight: bfloat16 [16384, 1024], P('row', 'col'), may hold values from -0.25 to 0.25
- out_weight: bfloat16 [16384, 16384], P('col', 'row'), may hold values from -0.046875 to 0.046875
- kv_cache: bfloat16 [8, 2, 4096, 256], P(None, None, ('row', 'col')), may hold values from -72 to 72
- cache_lengths: int32 [2], replicated, may hold values from 1024 to 4096, as said below
Outputs:
- layer_out: bfloat16 [1024, 16384], P('col', 'row')
The draws below stay inside these ranges and needn't reach their ends.
Inputs may be any that keep to these rules, and one draw needn't show every extreme that they name: `cache_lengths`: some sequence fills all 4096 slots.
All inputs are finite; a program needn't handle non-finite values.
Results may differ from the reference program's by a relative error of at most 0.019.
The reference program's roundings to bfloat16 on the way count: a program that leaves them out, or rounds other values in their place, can miss the bound.
Values may be sent and summed in bfloat16 or wider, within the bound.
No kernel may reach another device: no remote copies, remote signals or barrier semaphores. Data moves between devices by JAX's collectives and lax.ppermute only.
A program may use at most 64 MiB of HBM per device.

```python
import math
import jax
import jax.numpy as jnp
from jax import lax

D = 16384
HEADS = 128
KV_HEADS = 8
HEAD_DIM = 128
SEQS = 2
SPAN = 512
CACHE = 4096
TOKENS = 1024
N_COL = 16


def draw_residual(key, part):
    key_first = jax.random.fold_in(jax.random.fold_in(key, 23), 0)
    place = jnp.arange(D, dtype=jnp.float32) / (D - 1)
    column_scale = jnp.exp(math.log(0.6) + place * math.log(3.0))
    values = jnp.clip(jax.random.normal(key_first, (TOKENS, D), jnp.float32), -4.0, 4.0) * column_scale[None, :]
    return values.astype(jnp.bfloat16)


def draw_kv_cache(key, part):
    key_first, key_second = jax.random.split(jax.random.fold_in(key, 11), 2)
    array_shape = (KV_HEADS, SEQS, CACHE, HEAD_DIM)
    key_part = 2.0 * jnp.clip(jax.random.normal(key_first, array_shape, jnp.float32), -6.0, 6.0)
    value_part = 6.0 * jnp.clip(jax.random.normal(key_second, array_shape, jnp.float32), -6.0, 6.0)
    return jnp.concatenate([key_part, value_part], axis=-1).astype(jnp.bfloat16)


def draw_cache_lengths(key, part):
    key_first, key_second = jax.random.split(jax.random.fold_in(key, 7))
    lengths = jax.random.randint(key_first, (SEQS,), CACHE // 4, CACHE + 1)
    longest = jax.random.randint(key_second, (), 0, SEQS)
    return jnp.where(jnp.arange(SEQS) == longest, CACHE, lengths).astype(jnp.int32)


def shard_levels(key, shape, cuts, smallest, high):
    gain, own = 1.0, jax.random.fold_in(key, 6)
    for position, shards_of in cuts:
        steps = jnp.exp(jax.random.uniform(jax.random.fold_in(own, position), (shards_of,), jnp.float32, smallest / len(cuts), high / len(cuts)))
        gain = gain * jnp.repeat(steps, shape[position] // shards_of).reshape([-1 if axis == position else 1 for axis in range(len(shape))])
    return gain


def gaussian(stream_key, extent, width, reach, pieces=(), held_as=jnp.bfloat16):
    level = shard_levels(stream_key, extent, pieces, -0.22, 0.18) if pieces else 1.0
    values = jax.random.normal(stream_key, extent, jnp.float32) * width * level
    return jnp.minimum(jnp.maximum(values, -reach), reach).astype(held_as)


def setup_inputs(seed: int = 0) -> dict:
    arg_keys = jax.random.split(jax.random.key(seed), 9)
    residual = draw_residual(jax.random.fold_in(arg_keys[8], 71), 0)
    norm_gain = jnp.clip(1.0 + 0.1 * jax.random.normal(arg_keys[1], (D,), jnp.float32), 0.5, 1.5)
    query_weight = gaussian(arg_keys[2], (D, HEADS * HEAD_DIM), D ** -0.5, 0.046875, ((0, 8), (1, 16)))
    key_weight = gaussian(arg_keys[3], (D, KV_HEADS * HEAD_DIM), (D // 4) ** -0.5, 0.09375, ((0, 8), (1, 16)))
    value_weight = gaussian(arg_keys[4], (D, KV_HEADS * HEAD_DIM), (D // 36) ** -0.5, 0.25, ((0, 8), (1, 16)))
    out_weight = gaussian(arg_keys[5], (HEADS * HEAD_DIM, D), (HEADS * HEAD_DIM) ** -0.5, 0.046875, ((0, 16), (1, 8)))
    kv_cache = draw_kv_cache(jax.random.fold_in(arg_keys[8], 71), 0)
    cache_lengths = draw_cache_lengths(jax.random.fold_in(arg_keys[8], 71), 0)
    return {"residual": residual, "norm_gain": norm_gain, "query_weight": query_weight, "key_weight": key_weight, "value_weight": value_weight, "out_weight": out_weight, "kv_cache": kv_cache, "cache_lengths": cache_lengths}


ROPE_THETA = 500000.0
NORM_EPS = 1e-05

def rotate(vectors, positions):
    half_dim = vectors.shape[-1] // 2
    frequency = jnp.power(ROPE_THETA, -2.0 * jnp.arange(half_dim, dtype=jnp.float32) / vectors.shape[-1])
    angles = positions.astype(jnp.float32)[:, None] * frequency[None, :]
    cosine = jnp.cos(angles)[:, None, :]
    sine_part = jnp.sin(angles)[:, None, :]
    leading = vectors[..., :half_dim]
    second = vectors[..., half_dim:]
    return jnp.concatenate([leading * cosine - second * sine_part, second * cosine + leading * sine_part], axis=-1)

def reference(residual, norm_gain, query_weight, key_weight, value_weight, out_weight, kv_cache, cache_lengths):
    stream = residual.astype(jnp.float32)
    inverse_rms = lax.rsqrt(lax.optimization_barrier(jnp.mean(stream * stream, axis=1, keepdims=True)) + NORM_EPS)
    normed = (stream * inverse_rms * norm_gain[None, :]).astype(jnp.bfloat16)
    query_raw = jnp.dot(normed, query_weight, preferred_element_type=jnp.float32)
    new_keys_raw = jnp.dot(normed, key_weight, preferred_element_type=jnp.float32).astype(jnp.bfloat16)
    new_values = jnp.dot(normed, value_weight, preferred_element_type=jnp.float32).astype(jnp.bfloat16)
    offsets = jnp.arange(SPAN, dtype=jnp.int32)
    positions = (cache_lengths[:, None] + offsets[None, :]).reshape(TOKENS)
    queries = rotate(query_raw.reshape(TOKENS, HEADS, HEAD_DIM), positions).astype(jnp.bfloat16)
    new_keys = rotate(new_keys_raw.astype(jnp.float32).reshape(TOKENS, KV_HEADS, HEAD_DIM), positions).astype(jnp.bfloat16)
    new_values = new_values.reshape(TOKENS, KV_HEADS, HEAD_DIM)
    group_size = HEADS // KV_HEADS
    scale = 1.0 / math.sqrt(HEAD_DIM)
    key_index = jnp.arange(CACHE + SPAN, dtype=jnp.int32)
    query_pos = jnp.tile(jnp.arange(SPAN, dtype=jnp.int32), group_size)

    def attend(pair_index):
        sequence = pair_index // KV_HEADS
        kv_index = pair_index % KV_HEADS
        zero_index = jnp.zeros((), jnp.int32)
        picked = lax.dynamic_slice(queries, (sequence * SPAN, kv_index * group_size, zero_index), (SPAN, group_size, HEAD_DIM))
        picked = jnp.transpose(picked, (1, 0, 2)).reshape(group_size * SPAN, HEAD_DIM)
        cache_rows = kv_cache[kv_index, sequence]
        span_keys = lax.dynamic_slice(new_keys, (sequence * SPAN, kv_index, zero_index), (SPAN, 1, HEAD_DIM))[:, 0, :]
        span_values = lax.dynamic_slice(new_values, (sequence * SPAN, kv_index, zero_index), (SPAN, 1, HEAD_DIM))[:, 0, :]
        key_rows = jnp.concatenate([cache_rows[:, :HEAD_DIM], span_keys], axis=0)
        value_rows = jnp.concatenate([cache_rows[:, HEAD_DIM:], span_values], axis=0)
        length = cache_lengths[sequence]
        scores = jnp.einsum('qd,kd->qk', picked.astype(jnp.float32), key_rows.astype(jnp.float32)) * scale
        visible = jnp.where(key_index[None, :] < CACHE, (key_index < length)[None, :], key_index[None, :] - CACHE <= query_pos[:, None])
        scores = jnp.where(visible, scores, -jnp.inf)
        row_max = lax.optimization_barrier(jnp.max(scores, axis=1, keepdims=True))
        weights = jnp.exp(scores - row_max)
        totals = lax.optimization_barrier(jnp.sum(weights, axis=1, keepdims=True))
        mixture = jnp.dot(weights.astype(jnp.bfloat16), value_rows, preferred_element_type=jnp.float32) / totals
        return mixture.astype(jnp.bfloat16).reshape(group_size, SPAN, HEAD_DIM)
    results = lax.map(attend, jnp.arange(SEQS * KV_HEADS, dtype=jnp.int32))
    attended = results.reshape(SEQS, KV_HEADS, group_size, SPAN, HEAD_DIM)
    attended = jnp.transpose(attended, (0, 3, 1, 2, 4)).reshape(TOKENS, HEADS * HEAD_DIM)
    group_cols = HEADS * HEAD_DIM // N_COL
    branch = jnp.zeros((TOKENS, D), jnp.float32)
    for column in range(N_COL):
        partial_sum = jnp.dot(attended[:, column * group_cols:(column + 1) * group_cols], out_weight[column * group_cols:(column + 1) * group_cols, :], preferred_element_type=jnp.float32)
        rounded = lax.optimization_barrier(partial_sum.astype(jnp.bfloat16)).astype(jnp.float32)
        branch = branch + rounded
    return (stream + branch).astype(jnp.bfloat16)
```

```python
import math

import jax
import jax.numpy as jnp
from jax import lax
from jax.sharding import PartitionSpec as P

D = 16384
KV_HEADS = 8
HEAD_DIM = 128
SEQS = 2
SPAN = 512
CACHE = 4096


ROPE_THETA = 500000.0
NORM_EPS = 1e-05


def partner_2(value, axis, bit):
    mask = 2**bit
    pairs = [(source, source ^ mask) for source in range(lax.axis_size(axis))]
    return lax.ppermute(value, axis, pairs)


def rotate(vectors, positions):
    half_dim = vectors.shape[-1] // 2
    frequency = jnp.power(
        ROPE_THETA, -2.0 * jnp.arange(half_dim, dtype=jnp.float32) / vectors.shape[-1]
    )
    angles = positions.astype(jnp.float32)[:, None] * frequency[None, :]
    cosine = jnp.cos(angles)[:, None, :]
    sine_part = jnp.sin(angles)[:, None, :]
    leading = vectors[..., :half_dim]
    second = vectors[..., half_dim:]
    return jnp.concatenate(
        [leading * cosine - second * sine_part, second * cosine + leading * sine_part], axis=-1
    )


def body(
    residual, norm_gain, query_weight, key_weight, value_weight, out_weight, kv_cache, cache_lengths
):
    row_devices = lax.axis_size("row")
    col_devices = lax.axis_size("col")
    row_index = lax.axis_index("row")
    col_index = lax.axis_index("col")
    tok_col = residual.shape[0]
    tok_row = tok_col * col_devices // row_devices
    query_cols = query_weight.shape[1]
    key_cols = key_weight.shape[1]
    heads_dev = query_cols // HEAD_DIM
    group_cols = col_devices // KV_HEADS
    group_rows = row_devices // SEQS
    slots = kv_cache.shape[2]
    by_seq = jnp.transpose(kv_cache, (1, 0, 2, 3))
    send = jnp.repeat(jnp.repeat(by_seq, group_rows, axis=0), group_cols, axis=1)
    send = send.reshape(row_devices * col_devices, slots, kv_cache.shape[3])
    cache_rows = lax.all_to_all(send, ("row", "col"), 0, 0, tiled=True)
    cache_rows = cache_rows.reshape(row_devices * col_devices * slots, kv_cache.shape[3])
    gathered = lax.all_gather(residual, "col", axis=0, tiled=True)
    stream = residual.astype(jnp.float32)
    squares = lax.psum(jnp.sum(stream * stream, axis=1), "row")
    inverse_rms = lax.rsqrt(squares / D + NORM_EPS)
    inverse_rms = lax.all_gather(inverse_rms, "col", axis=0, tiled=True)
    normed = (gathered.astype(jnp.float32) * inverse_rms[:, None] * norm_gain[None, :]).astype(
        jnp.bfloat16
    )
    partial = jnp.concatenate(
        [
            jnp.dot(normed, query_weight, preferred_element_type=jnp.float32).astype(jnp.bfloat16),
            jnp.dot(normed, key_weight, preferred_element_type=jnp.float32).astype(jnp.bfloat16),
            jnp.dot(normed, value_weight, preferred_element_type=jnp.float32).astype(jnp.bfloat16),
        ],
        axis=1,
    )
    pieces = lax.all_to_all(partial, "row", 0, 0, tiled=True)
    summed = pieces.reshape(row_devices, tok_row, -1).astype(jnp.float32).sum(axis=0)
    first_row = row_index * tok_row
    sequence = first_row // SPAN
    offset = first_row % SPAN
    length = jnp.sum(jnp.where(jnp.arange(SEQS, dtype=jnp.int32) == sequence, cache_lengths, 0))
    positions = length + offset + jnp.arange(tok_row, dtype=jnp.int32)
    queries = rotate(
        summed[:, :query_cols].reshape(tok_row, heads_dev, HEAD_DIM), positions
    ).astype(jnp.bfloat16)
    new_pairs = summed[:, query_cols:].astype(jnp.bfloat16)
    head_pieces = new_pairs[:, None, :]
    bit_number = 0
    partner = partner_2(head_pieces, "col", bit_number)
    upper = col_index // (1 << bit_number) % 2 == 1
    head_pieces = jnp.where(
        upper,
        jnp.concatenate([partner, head_pieces], axis=1),
        jnp.concatenate([head_pieces, partner], axis=1),
    )
    own_keys = head_pieces[:, :, :key_cols].reshape(tok_row, HEAD_DIM)
    own_values = head_pieces[:, :, key_cols:].reshape(tok_row, HEAD_DIM)
    own_keys = rotate(own_keys.astype(jnp.float32)[:, None, :], positions)[:, 0, :].astype(
        jnp.bfloat16
    )
    pair_rows = jnp.concatenate([own_keys, own_values], axis=1)
    row_group = row_devices // SEQS
    for bit_number in range(row_group.bit_length() - 1):
        partner = partner_2(pair_rows, "row", bit_number)
        upper = row_index // (1 << bit_number) % 2 == 1
        pair_rows = jnp.where(
            upper,
            jnp.concatenate([partner, pair_rows], axis=0),
            jnp.concatenate([pair_rows, partner], axis=0),
        )
    key_rows = jnp.concatenate([cache_rows[:, :HEAD_DIM], pair_rows[:, :HEAD_DIM]], axis=0)
    value_rows = jnp.concatenate([cache_rows[:, HEAD_DIM:], pair_rows[:, HEAD_DIM:]], axis=0)
    flat_query = jnp.transpose(queries, (1, 0, 2)).reshape(heads_dev * tok_row, HEAD_DIM)
    total_rows = heads_dev * tok_row
    block_rows = math.gcd(total_rows, 512)
    key_index = jnp.arange(CACHE + SPAN, dtype=jnp.int32)
    scale = 1.0 / math.sqrt(HEAD_DIM)

    def attend(block_index):
        begin_row = block_index * block_rows
        picked = lax.dynamic_slice_in_dim(flat_query, begin_row, block_rows, 0)
        query_pos = offset + (begin_row + jnp.arange(block_rows, dtype=jnp.int32)) % tok_row
        scores = (
            jnp.einsum("qd,kd->qk", picked, key_rows, preferred_element_type=jnp.float32) * scale
        )
        visible = jnp.where(
            key_index[None, :] < CACHE,
            (key_index < length)[None, :],
            key_index[None, :] - CACHE <= query_pos[:, None],
        )
        scores = jnp.where(visible, scores, -jnp.inf)
        row_max = jnp.max(scores, axis=1, keepdims=True)
        weights = jnp.exp(scores - row_max)
        totals = jnp.sum(weights, axis=1, keepdims=True)
        mixture = (
            jnp.dot(weights.astype(jnp.bfloat16), value_rows, preferred_element_type=jnp.float32)
            / totals
        )
        return mixture.astype(jnp.bfloat16)

    blocks = lax.map(attend, jnp.arange(total_rows // block_rows, dtype=jnp.int32))
    attended = jnp.transpose(blocks.reshape(heads_dev, tok_row, HEAD_DIM), (1, 0, 2)).reshape(
        tok_row, query_cols
    )
    head_rows = lax.all_gather(attended, "row", axis=0, tiled=True)
    picked = head_rows
    products = jnp.dot(picked, out_weight, preferred_element_type=jnp.float32).astype(jnp.bfloat16)
    products = lax.all_to_all(products, "col", 0, 0, tiled=True)
    branch = products.reshape(col_devices, tok_col, -1).astype(jnp.float32).sum(axis=0)
    return (residual.astype(jnp.float32) + branch).astype(jnp.bfloat16)


def solution(mesh):
    return jax.shard_map(
        body,
        mesh=mesh,
        in_specs=(
            P("col", "row"),
            P("row"),
            P("row", "col"),
            P("row", "col"),
            P("row", "col"),
            P("col", "row"),
            P(None, None, ("row", "col"), None),
            P(),
        ),
        out_specs=P("col", "row"),
        check_vma=False,
    )
```
